256 devices in a mesh: ctx: 64 (over y, z, core), tp: 4 (over x).
Axes of the slice: x: 4, y: 4, z: 8, core: 2. Of those that a mesh axis runs over, the one named last changes fastest.
Arguments:
- queries: bfloat16 [32768, 4096], P('ctx', 'tp'), may hold values from -160 to 160
- keys: bfloat16 [32768, 512], P('ctx', 'tp'), may hold values from -5 to 5
- values: bfloat16 [32768, 512], P('ctx', 'tp'), may hold values from -6.5 to 6.5
- evicted: int32 [32768, 4], P('ctx', 'tp'), may hold values 0 or 1
- block_lists: int32 [256, 2], P('ctx'), may hold values from 0 to 6, as said below
- map_query: bfloat16 [4, 128, 64], P('tp'), may hold values from -0.5 to 0.5
- map_key: bfloat16 [4, 128, 64], P('tp'), may hold values from -0.5 to 0.5
- state_gain: float32 [4], P('tp'), may hold values from 0.001953125 to 0.0078125
- out_weight: bfloat16 [4096, 8192], P('tp', 'ctx'), may hold values from -0.09375 to 0.09375
Outputs:
- layer_out: bfloat16 [32768, 8192], P('ctx', 'tp')
The draws below stay inside these ranges and needn't reach their ends.
Inputs may be any that keep to these rules, and one draw needn't show every extreme that they name: `block_lists`: query block b with local index i = b % (4) lists entry 0 = 4 + i - 1 and entry 1 in 0 to 4 + i - 2, so the two entries differ and lie before the diagonal block.
All inputs are finite; a program needn't handle non-finite values. No bound on the sum of `evicted` on one device may be relied on, other than what follows from the above.
Results may differ from the reference program's by a relative error of at most 0.012.
Values may be sent and summed in bfloat16 or wider, within the bound.
No kernel may reach another device: no remote copies, remote signals or barrier semaphores. Data moves between devices by JAX's collectives and lax.ppermute only.
A program may use at most 128 MiB of HBM per device.

```python
import math
import jax
import jax.numpy as jnp
from jax import lax

D = 8192
HD = 128
KVH = 4
GROUP = 8
QH = 32
R = 64
TOK_DEV = 512
QB = 128
TOKENS = 32768
QBLOCKS = 256
N_CTX = 64
N_TP = 4


def joint_heads(key):
    raw_keys = jnp.clip(jax.random.normal(jax.random.fold_in(key, 11), (TOKENS, KVH * HD), jnp.float32), -5.0, 5.0)
    raw_queries = jnp.clip(jax.random.normal(jax.random.fold_in(key, 12), (TOKENS, QH * HD), jnp.float32), -5.0, 5.0)
    return (raw_queries, raw_keys)


def draw_queries(key, part):
    return joint_heads(key)[0].astype(jnp.bfloat16)


def draw_keys(key, part):
    return joint_heads(key)[1].astype(jnp.bfloat16)


def draw_values(key, part):
    noise = jnp.clip(jax.random.normal(jax.random.fold_in(key, 31), (TOKENS, KVH * HD), jnp.float32), -5.0, 5.0)
    means = jax.random.uniform(jax.random.fold_in(key, 32), (TOKENS // TOK_DEV, KVH * HD), jnp.float32, -1.5, 1.5)
    return (noise + jnp.repeat(means, TOK_DEV, axis=0)).astype(jnp.bfloat16)


def draw_block_lists(key, part):
    count = TOKENS // QB
    blocks_dev = TOK_DEV // QB
    local = jnp.arange(count, dtype=jnp.int32) % blocks_dev
    recent = blocks_dev + local - 1
    other = jax.random.randint(jax.random.fold_in(key, 21), (count,), 0, recent, dtype=jnp.int32)
    other = jnp.where(jnp.arange(count) == 0, 0, other)
    return jnp.stack([recent, other], axis=1).astype(jnp.int32)


def set_ends(drawn, key, least, largest):
    spot = [jax.random.randint(jax.random.fold_in(key, axis), (), 0, length) for axis, length in enumerate(drawn.shape)]
    longest = drawn.shape.index(max(drawn.shape))
    next_to = spot[:longest] + [(spot[longest] + 1) % drawn.shape[longest]] + spot[longest + 1:]
    return drawn.at[tuple(spot)].set(least).at[tuple(next_to)].set(largest)


def level_of(stream_key, shape, split, low, high):
    gain = 1.0
    for axis_at, shards_of in split:
        draws = jax.random.uniform(jax.random.fold_in(jax.random.fold_in(stream_key, 6), axis_at), (shards_of,), jnp.float32, low / len(split), high / len(split))
        gain = gain * jnp.repeat(jnp.exp(draws), shape[axis_at] // shards_of).reshape((-1,) + (1,) * (len(shape) - 1 - axis_at))
    return gain


def gaussian(rng, shape, width, most, pieces=(), held_as=jnp.bfloat16):
    drawn = width * jax.random.normal(rng, shape, jnp.float32)
    if pieces:
        drawn = drawn * level_of(rng, shape, pieces, -0.22, 0.18)
    return jnp.clip(drawn, -most, most).astype(held_as)


def setup_inputs(seed: int = 0) -> dict:
    key_list = jax.random.split(jax.random.key(seed), 10)
    queries = draw_queries(jax.random.fold_in(key_list[9], 71), 0)
    keys = draw_keys(jax.random.fold_in(key_list[9], 71), 0)
    values = draw_values(jax.random.fold_in(key_list[9], 71), 0)
    evicted = set_ends((jax.random.randint(key_list[3], (TOKENS, KVH), 0, 2) < 1).astype(jnp.int32), jax.random.fold_in(key_list[3], 1), 0, 1)
    block_lists = draw_block_lists(jax.random.fold_in(key_list[9], 71), 0)
    map_query = gaussian(key_list[5], (KVH, HD, R), HD ** -0.5, 0.5, ((0, 4),))
    map_key = gaussian(key_list[6], (KVH, HD, R), HD ** -0.5, 0.5, ((0, 4),))
    state_gain = jnp.clip(jnp.exp(math.log(0.0078125) - 1.3862944 * jax.random.uniform(key_list[7], (KVH,), jnp.float32) ** level_of(key_list[7], (KVH,), ((0, 4),), -0.2, 0.2)), 0.001953125, 0.0078125)
    out_weight = gaussian(key_list[8], (QH * HD, D), (QH * HD) ** -0.5, 0.09375, ((0, 4), (1, 64)))
    return {"queries": queries, "keys": keys, "values": values, "evicted": evicted, "block_lists": block_lists, "map_query": map_query, "map_key": map_key, "state_gain": state_gain, "out_weight": out_weight}


def feature(inputs, kernel):
    return jax.nn.elu(jnp.dot(inputs, kernel, preferred_element_type=jnp.float32)) + 1.0


def reference(queries, keys, values, evicted, block_lists, map_query, map_key, state_gain, out_weight):
    blocks_dev = TOK_DEV // QB
    highest = lax.Precision.HIGHEST
    group_cols = []
    for group in range(KVH):
        key_group = keys[:, group * HD:(group + 1) * HD]
        value_group = values[:, group * HD:(group + 1) * HD]
        query_group = queries[:, group * GROUP * HD:(group + 1) * GROUP * HD].reshape(TOKENS, GROUP, HD)
        key_feats = feature(key_group, map_key[group]) * evicted[:, group:group + 1].astype(jnp.float32)
        feat_blocks = key_feats.reshape(N_CTX, TOK_DEV, R)
        value_blocks = value_group.astype(jnp.float32).reshape(N_CTX, TOK_DEV, HD)
        totals = jnp.einsum("ctr,cth->crh", feat_blocks, value_blocks, precision=highest)
        counts = jnp.sum(feat_blocks, axis=1)
        states = jnp.cumsum(jnp.concatenate([jnp.zeros((1, R, HD), jnp.float32), totals[:-1]], axis=0), axis=0)
        norms = jnp.cumsum(jnp.concatenate([jnp.zeros((1, R), jnp.float32), counts[:-1]], axis=0), axis=0)

        def one_block(index):
            device = index // blocks_dev
            local = index % blocks_dev
            query = lax.dynamic_slice_in_dim(query_group, (index * QB).astype(jnp.int32), QB, 0)
            chosen = jnp.concatenate([block_lists[index], (blocks_dev + local)[None]]).astype(jnp.int32)
            positions = ((device - 1) * TOK_DEV + chosen * QB)[:, None] + jnp.arange(QB, dtype=jnp.int32)[None, :]
            positions = positions.reshape(-1).astype(jnp.int32)
            rows_safe = jnp.maximum(positions, 0)
            key_rows = jnp.take(key_group, rows_safe, axis=0)
            value_rows = jnp.take(value_group, rows_safe, axis=0)
            query_pos = index * QB + jnp.arange(QB, dtype=jnp.int32)
            valid = (positions[None, :] >= 0) & (positions[None, :] <= query_pos[:, None])
            scores = jnp.einsum("qhd,kd->hqk", query.astype(jnp.float32), key_rows.astype(jnp.float32)) * (HD ** -0.5)
            scores = jnp.where(valid[None, :, :], scores, -jnp.inf)
            top = jnp.max(scores, axis=2)
            weights = jnp.exp(scores - top[:, :, None])
            total = jnp.sum(weights, axis=2)
            probs = weights.astype(jnp.bfloat16)
            numer = jnp.einsum("hqk,kd->hqd", probs.astype(jnp.float32), value_rows.astype(jnp.float32))
            query_feats = feature(query, map_query[group])
            reads = jnp.einsum("qhr,rd->hqd", query_feats, states[device], precision=highest)
            mass = jnp.einsum("qhr,r->hq", query_feats, norms[device], precision=highest)
            damping = jnp.exp(-top) * state_gain[group]
            mixed = (numer + damping[:, :, None] * reads) / (total + damping * mass)[:, :, None]
            return jnp.transpose(mixed, (1, 0, 2)).reshape(QB, GROUP * HD).astype(jnp.bfloat16)

        result = lax.map(one_block, jnp.arange(QBLOCKS, dtype=jnp.int32))
        group_cols.append(result.reshape(TOKENS, GROUP * HD))
    attn = jnp.concatenate(group_cols, axis=1)
    heads_dev = (QH // N_TP) * HD

    def project(block):
        summed = jnp.zeros((TOK_DEV, D), jnp.float32)
        for member in range(N_TP):
            part_rows = block[:, member * heads_dev:(member + 1) * heads_dev]
            partial_value = jnp.dot(part_rows, out_weight[member * heads_dev:(member + 1) * heads_dev], preferred_element_type=jnp.float32).astype(jnp.bfloat16)
            summed = summed + lax.optimization_barrier(partial_value).astype(jnp.float32)
        return summed.astype(jnp.bfloat16)

    layer_out = lax.map(project, attn.reshape(N_CTX, TOK_DEV, QH * HD))
    return layer_out.reshape(TOKENS, D)
```

```python
import jax
import jax.numpy as jnp
from jax import lax
from jax.sharding import Mesh
from jax.sharding import PartitionSpec as P

CTX = ("ctx_0", "ctx_1", "ctx_2")


def passed_along(block, axis, distance):
    devices = range(lax.axis_size(axis))
    route = [(i - distance, i) for i in devices if i - distance in devices]
    return lax.ppermute(block, axis, route)


def neutral_like(shard, identity):
    return jax.tree.map(
        lambda a, e: jnp.broadcast_to(jnp.asarray(e, a.dtype), a.shape), shard, identity
    )


def all_in_one(shard, axis):
    leaves = jax.tree.leaves(shard)
    order = sorted(range(len(leaves)), key=lambda k: -leaves[k].size)
    width = (1, *leaves[order[0]].shape)[-1]
    lines = [
        jnp.pad(leaves[k].reshape(-1), (0, -leaves[k].size % width)).reshape(-1, width)
        for k in order
    ]
    both, at, found = (lax.all_gather(jnp.concatenate(lines), axis), 0, {})
    for k, line in zip(order, lines):
        slab = both[:, at : at + len(line)].reshape(len(both), -1)
        found[k] = slab[:, : leaves[k].size].reshape(-1, *leaves[k].shape)
        at += len(line)
    numbers = iter(range(len(leaves)))
    return jax.tree.map(lambda _: found[next(numbers)], shard)


def carried_in(shard, axes, combine, identity):
    before = start = neutral_like(shard, identity)
    running = shard
    for axis in reversed(axes):
        devices, here = (lax.axis_size(axis), lax.axis_index(axis))
        pieces = all_in_one(
            jax.tree.map(
                lambda part, kind: part.astype(kind), running, (jnp.bfloat16, jnp.bfloat16)
            ),
            axis,
        )
        inside, running = (start, start)
        for k in range(devices):
            passed = k < here
            running = combine(
                running, jax.tree.map(lambda part, own: part[k].astype(own.dtype), pieces, shard)
            )
            inside = jax.tree.map(lambda new, old: jnp.where(passed, new, old), running, inside)
        before = combine(inside, before)
    return before


def feature(inputs, kernel):
    return jax.nn.elu(jnp.dot(inputs, kernel, preferred_element_type=jnp.float32)) + 1.0


def add_pair(earlier, later):
    return (earlier[0] + later[0], earlier[1] + later[1])


def body(queries, keys, values, evicted, block_lists, map_query, map_key, state_gain, out_weight):
    tok_rows = keys.shape[0]
    groups_here = map_key.shape[0]
    head_dim = map_key.shape[1]
    blocks_dev = block_lists.shape[0]
    block_rows = tok_rows // blocks_dev
    group_size = queries.shape[1] // (groups_here * head_dim)
    highest = lax.Precision.HIGHEST
    device = lax.axis_index(CTX)
    width_kv = groups_here * head_dim
    neighbour = passed_along(jnp.concatenate([keys, values], axis=1), CTX, 1)
    left_keys = neighbour[:, :width_kv]
    left_values = neighbour[:, width_kv:]
    group = 0
    key_feats = feature(keys, map_key[group]) * evicted.astype(jnp.float32)
    state_terms = [
        jnp.einsum("tr,th->rh", key_feats, values.astype(jnp.float32), precision=highest)
    ]
    norm_terms = [jnp.sum(key_feats, axis=0)]
    totals = jnp.stack(state_terms)
    counts = jnp.stack(norm_terms)
    states, norms = carried_in(
        (totals, counts), CTX, add_pair, (jnp.zeros_like(totals), jnp.zeros_like(counts))
    )
    scale = head_dim ** (-0.5)
    offsets = jnp.arange(block_rows, dtype=jnp.int32)
    group = 0
    window_keys = jnp.concatenate([left_keys, keys], axis=0).reshape(
        2 * blocks_dev, block_rows, head_dim
    )
    window_values = jnp.concatenate([left_values, values], axis=0).reshape(
        2 * blocks_dev, block_rows, head_dim
    )
    query_group = queries.reshape(tok_rows, group_size, head_dim)
    query_feats = feature(query_group, map_query[group])
    reads = jnp.einsum("qhr,rd->qhd", query_feats, states[group], precision=highest)
    mass = jnp.einsum("qhr,r->qh", query_feats, norms[group], precision=highest)
    row_pieces = []
    for local in range(blocks_dev):
        chosen = jnp.concatenate(
            [block_lists[local], jnp.full((1,), blocks_dev + local, jnp.int32)]
        )
        key_rows = jnp.take(window_keys, chosen, axis=0).reshape(-1, head_dim)
        value_rows = jnp.take(window_values, chosen, axis=0).reshape(-1, head_dim)
        positions = (
            ((device - 1) * tok_rows + chosen * block_rows)[:, None] + offsets[None, :]
        ).reshape(-1)
        query_pos = device * tok_rows + local * block_rows + offsets
        valid = (positions[None, :] >= 0) & (positions[None, :] <= query_pos[:, None])
        rows_here = slice(local * block_rows, (local + 1) * block_rows)
        query = query_group[rows_here]
        scores = (
            jnp.einsum("qhd,kd->qhk", query, key_rows, preferred_element_type=jnp.float32) * scale
        )
        scores = jnp.where(valid[:, None, :], scores, -jnp.inf)
        top = jnp.max(scores, axis=2)
        weights = jnp.exp(scores - top[:, :, None])
        total = jnp.sum(weights, axis=2)
        probs = weights.astype(jnp.bfloat16)
        numer = jnp.einsum("qhk,kd->qhd", probs, value_rows, preferred_element_type=jnp.float32)
        damping = jnp.exp(-top) * state_gain[group]
        mixed = (numer + damping[:, :, None] * reads[rows_here]) / (
            total + damping * mass[rows_here]
        )[:, :, None]
        row_pieces.append(mixed.reshape(block_rows, group_size * head_dim).astype(jnp.bfloat16))
    group_cols = jnp.concatenate(row_pieces, axis=0)
    n_tp = lax.axis_size("tp")
    swap = [
        (rows * n_tp + group, ((rows - group) % n_tp) * n_tp + rows)
        for group in range(n_tp)
        for rows in range(n_tp)
    ]
    moved = lax.ppermute(out_weight, ("ctx_0", "tp"), swap)
    gathered = lax.all_gather(moved, CTX, axis=1, tiled=True)
    width = gathered.shape[1] // n_tp
    summed = None
    for shift in range(n_tp):
        if shift == 0:
            rows_in = group_cols
        else:
            rows_in = lax.ppermute(
                group_cols, "tp", [(i, (i + shift) % n_tp) for i in range(n_tp)]
            )
        term = jnp.dot(
            rows_in,
            gathered[:, shift * width : (shift + 1) * width],
            preferred_element_type=jnp.float32,
        )
        summed = term if summed is None else summed + term
    return summed.astype(jnp.bfloat16)


def solution(mesh):
    finer = Mesh(mesh.devices.reshape(4, 8, 2, mesh.shape["tp"]), ("ctx_0", "ctx_1", "ctx_2", "tp"))
    placed = (
        P(CTX, "tp"),
        P(CTX, "tp"),
        P(CTX, "tp"),
        P(CTX, "tp"),
        P(CTX, None),
        P("tp", None, None),
        P("tp", None, None),
        P("tp"),
        P("tp", CTX),
    )
    return jax.shard_map(body, mesh=finer, in_specs=placed, out_specs=P(CTX, "tp"), check_vma=False)
```

```python
import jax
import jax.numpy as jnp
from jax import lax
from jax.sharding import Mesh
from jax.sharding import PartitionSpec as P

CTX = ("ctx_0", "ctx_1", "ctx_2")


def passed_along(block, axis, distance):
    devices = range(lax.axis_size(axis))
    route = [(i - distance, i) for i in devices if i - distance in devices]
    return lax.ppermute(block, axis, route)


def neutral_like(shard, identity):
    return jax.tree.map(
        lambda a, e: jnp.broadcast_to(jnp.asarray(e, a.dtype), a.shape), shard, identity
    )


def all_in_one(shard, axis):
    leaves = jax.tree.leaves(shard)
    order = sorted(range(len(leaves)), key=lambda k: -leaves[k].size)
    width = (1, *leaves[order[0]].shape)[-1]
    lines = [
        jnp.pad(leaves[k].reshape(-1), (0, -leaves[k].size % width)).reshape(-1, width)
        for k in order
    ]
    both, at, found = (lax.all_gather(jnp.concatenate(lines), axis), 0, {})
    for k, line in zip(order, lines):
        slab = both[:, at : at + len(line)].reshape(len(both), -1)
        found[k] = slab[:, : leaves[k].size].reshape(-1, *leaves[k].shape)
        at += len(line)
    numbers = iter(range(len(leaves)))
    return jax.tree.map(lambda _: found[next(numbers)], shard)


def carried_in(shard, axes, combine, identity):
    before = start = neutral_like(shard, identity)
    running = shard
    for axis in reversed(axes):
        devices, here = (lax.axis_size(axis), lax.axis_index(axis))
        pieces = all_in_one(
            jax.tree.map(
                lambda part, kind: part.astype(kind), running, (jnp.bfloat16, jnp.bfloat16)
            ),
            axis,
        )
        inside, running = (start, start)
        for k in range(devices):
            passed = k < here
            running = combine(
                running, jax.tree.map(lambda part, own: part[k].astype(own.dtype), pieces, shard)
            )
            inside = jax.tree.map(lambda new, old: jnp.where(passed, new, old), running, inside)
        before = combine(inside, before)
    return before


def feature(inputs, kernel):
    return jax.nn.elu(jnp.dot(inputs, kernel, preferred_element_type=jnp.float32)) + 1.0


def add_pair(earlier, later):
    return (earlier[0] + later[0], earlier[1] + later[1])


def body(queries, keys, values, evicted, block_lists, map_query, map_key, state_gain, out_weight):
    tok_rows = keys.shape[0]
    groups_here = map_key.shape[0]
    head_dim = map_key.shape[1]
    blocks_dev = block_lists.shape[0]
    block_rows = tok_rows // blocks_dev
    group_size = queries.shape[1] // (groups_here * head_dim)
    highest = lax.Precision.HIGHEST
    device = lax.axis_index(CTX)
    width_kv = groups_here * head_dim
    neighbour = passed_along(jnp.concatenate([keys, values], axis=1), CTX, 1)
    left_keys = neighbour[:, :width_kv]
    left_values = neighbour[:, width_kv:]
    group = 0
    key_feats = feature(keys, map_key[group]) * evicted.astype(jnp.float32)
    state_terms = [
        jnp.einsum("tr,th->rh", key_feats, values.astype(jnp.float32), precision=highest)
    ]
    norm_terms = [jnp.sum(key_feats, axis=0)]
    totals = jnp.stack(state_terms)
    counts = jnp.stack(norm_terms)
    packed = jnp.concatenate(
        [totals[0], jnp.pad(counts, ((0, 0), (0, totals.shape[2] - counts.shape[1])))], axis=0
    )
    packed = packed.astype(jnp.float32)
    n_ctx = lax.axis_size(CTX)
    running = packed
    distance = 1
    while distance < n_ctx:
        arrived = lax.ppermute(
            running, CTX, [(i, i + distance) for i in range(n_ctx - distance)]
        )
        running = running + arrived
        distance *= 2
    before = running - packed
    states = before[None, : totals.shape[1]]
    norms = before[None, totals.shape[1], : counts.shape[1]]
    scale = head_dim ** (-0.5)
    offsets = jnp.arange(block_rows, dtype=jnp.int32)
    group = 0
    window_keys = jnp.concatenate([left_keys, keys], axis=0).reshape(
        2 * blocks_dev, block_rows, head_dim
    )
    window_values = jnp.concatenate([left_values, values], axis=0).reshape(
        2 * blocks_dev, block_rows, head_dim
    )
    query_group = queries.reshape(tok_rows, group_size, head_dim)
    query_feats = feature(query_group, map_query[group])
    reads = jnp.einsum("qhr,rd->qhd", query_feats, states[group], precision=highest)
    mass = jnp.einsum("qhr,r->qh", query_feats, norms[group], precision=highest)
    row_pieces = []
    for local in range(blocks_dev):
        chosen = jnp.concatenate(
            [block_lists[local], jnp.full((1,), blocks_dev + local, jnp.int32)]
        )
        key_rows = jnp.take(window_keys, chosen, axis=0).reshape(-1, head_dim)
        value_rows = jnp.take(window_values, chosen, axis=0).reshape(-1, head_dim)
        positions = (
            ((device - 1) * tok_rows + chosen * block_rows)[:, None] + offsets[None, :]
        ).reshape(-1)
        query_pos = device * tok_rows + local * block_rows + offsets
        valid = (positions[None, :] >= 0) & (positions[None, :] <= query_pos[:, None])
        rows_here = slice(local * block_rows, (local + 1) * block_rows)
        query = query_group[rows_here]
        scores = (
            jnp.einsum("qhd,kd->qhk", query, key_rows, preferred_element_type=jnp.float32) * scale
        )
        scores = jnp.where(valid[:, None, :], scores, -jnp.inf)
        top = jnp.max(scores, axis=2)
        weights = jnp.exp(scores - top[:, :, None])
        total = jnp.sum(weights, axis=2)
        probs = weights.astype(jnp.bfloat16)
        numer = jnp.einsum("qhk,kd->qhd", probs, value_rows, preferred_element_type=jnp.float32)
        damping = jnp.exp(-top) * state_gain[group]
        mixed = (numer + damping[:, :, None] * reads[rows_here]) / (
            total + damping * mass[rows_here]
        )[:, :, None]
        row_pieces.append(mixed.reshape(block_rows, group_size * head_dim).astype(jnp.bfloat16))
    group_cols = jnp.concatenate(row_pieces, axis=0)
    n_tp = lax.axis_size("tp")
    n_z = lax.axis_size("ctx_1")
    n_core = lax.axis_size("ctx_2")
    every = ("ctx_0", "ctx_1", "ctx_2", "tp")

    def flat(y, z, core, x):
        return ((y * n_z + z) * n_core + core) * n_tp + x

    swap = []
    for y in range(n_tp):
        for z in range(n_z):
            for core in range(n_core):
                for x in range(n_tp):
                    piece = z * n_core + core
                    swap.append(
                        (
                            flat(y, z, core, x),
                            flat((y - x) % n_tp, piece % n_z, piece // n_z, y),
                        )
                    )
    moved = lax.ppermute(out_weight, every, swap)
    own_half = lax.all_gather(moved, ("ctx_0", "ctx_1"), axis=1, tiled=True)
    own_half, _ = lax.optimization_barrier((own_half, group_cols))
    other_half = lax.ppermute(own_half, "ctx_2", [(0, 1), (1, 0)])
    width = own_half.shape[1] // n_tp
    rows_by_shift = [group_cols] + [
        lax.ppermute(group_cols, "tp", [(i, (i + shift) % n_tp) for i in range(n_tp)])
        for shift in range(1, n_tp)
    ]

    def project(half):
        summed = None
        for shift in range(n_tp):
            term = jnp.dot(
                rows_by_shift[shift],
                half[:, shift * width : (shift + 1) * width],
                preferred_element_type=jnp.float32,
            )
            summed = term if summed is None else summed + term
        return summed

    mine = project(own_half)
    theirs = project(other_half)
    core = lax.axis_index("ctx_2")
    halves = jnp.where(core == 0, jnp.stack([mine, theirs]), jnp.stack([theirs, mine]))
    return jnp.concatenate([halves[0], halves[1]], axis=1).astype(jnp.bfloat16)


def solution(mesh):
    finer = Mesh(mesh.devices.reshape(4, 8, 2, mesh.shape["tp"]), ("ctx_0", "ctx_1", "ctx_2", "tp"))
    placed = (
        P(CTX, "tp"),
        P(CTX, "tp"),
        P(CTX, "tp"),
        P(CTX, "tp"),
        P(CTX, None),
        P("tp", None, None),
        P("tp", None, None),
        P("tp"),
        P("tp", CTX),
    )
    return jax.shard_map(body, mesh=finer, in_specs=placed, out_specs=P(CTX, "tp"), check_vma=False)
```

```python
import jax
import jax.numpy as jnp
from jax import lax
from jax.sharding import Mesh
from jax.sharding import PartitionSpec as P

CTX = ("ctx_0", "ctx_1", "ctx_2")


def passed_along(block, axis, distance):
    devices = range(lax.axis_size(axis))
    route = [(i - distance, i) for i in devices if i - distance in devices]
    return lax.ppermute(block, axis, route)


def neutral_like(shard, identity):
    return jax.tree.map(
        lambda a, e: jnp.broadcast_to(jnp.asarray(e, a.dtype), a.shape), shard, identity
    )


def all_in_one(shard, axis):
    leaves = jax.tree.leaves(shard)
    order = sorted(range(len(leaves)), key=lambda k: -leaves[k].size)
    width = (1, *leaves[order[0]].shape)[-1]
    lines = [
        jnp.pad(leaves[k].reshape(-1), (0, -leaves[k].size % width)).reshape(-1, width)
        for k in order
    ]
    both, at, found = (lax.all_gather(jnp.concatenate(lines), axis), 0, {})
    for k, line in zip(order, lines):
        slab = both[:, at : at + len(line)].reshape(len(both), -1)
        found[k] = slab[:, : leaves[k].size].reshape(-1, *leaves[k].shape)
        at += len(line)
    numbers = iter(range(len(leaves)))
    return jax.tree.map(lambda _: found[next(numbers)], shard)


def carried_in(shard, axes, combine, identity):
    before = start = neutral_like(shard, identity)
    running = shard
    for axis in reversed(axes):
        devices, here = (lax.axis_size(axis), lax.axis_index(axis))
        pieces = all_in_one(
            jax.tree.map(
                lambda part, kind: part.astype(kind), running, (jnp.bfloat16, jnp.bfloat16)
            ),
            axis,
        )
        inside, running = (start, start)
        for k in range(devices):
            passed = k < here
            running = combine(
                running, jax.tree.map(lambda part, own: part[k].astype(own.dtype), pieces, shard)
            )
            inside = jax.tree.map(lambda new, old: jnp.where(passed, new, old), running, inside)
        before = combine(inside, before)
    return before


def feature(inputs, kernel):
    return jax.nn.elu(jnp.dot(inputs, kernel, preferred_element_type=jnp.float32)) + 1.0


def add_pair(earlier, later):
    return (earlier[0] + later[0], earlier[1] + later[1])


def body(queries, keys, values, evicted, block_lists, map_query, map_key, state_gain, out_weight):
    tok_rows = keys.shape[0]
    groups_here = map_key.shape[0]
    head_dim = map_key.shape[1]
    blocks_dev = block_lists.shape[0]
    block_rows = tok_rows // blocks_dev
    group_size = queries.shape[1] // (groups_here * head_dim)
    highest = lax.Precision.HIGHEST
    device = lax.axis_index(CTX)
    width_kv = groups_here * head_dim
    neighbour = passed_along(jnp.concatenate([keys, values], axis=1), CTX, 1)
    left_keys = neighbour[:, :width_kv]
    left_values = neighbour[:, width_kv:]
    group = 0
    key_feats = feature(keys, map_key[group]) * evicted.astype(jnp.float32)
    state_terms = [
        jnp.einsum("tr,th->rh", key_feats, values.astype(jnp.float32), precision=highest)
    ]
    norm_terms = [jnp.sum(key_feats, axis=0)]
    totals = jnp.stack(state_terms)
    counts = jnp.stack(norm_terms)
    packed = jnp.concatenate(
        [totals[0], jnp.pad(counts, ((0, 0), (0, totals.shape[2] - counts.shape[1])))], axis=0
    )
    every_state = lax.all_gather(packed.astype(jnp.float32), CTX, axis=0)
    earlier = jnp.arange(every_state.shape[0], dtype=jnp.int32) < device
    before = jnp.sum(jnp.where(earlier[:, None, None], every_state, 0.0), axis=0)
    states = before[None, : totals.shape[1]]
    norms = before[None, totals.shape[1], : counts.shape[1]]
    out_weight, _ = lax.optimization_barrier((out_weight, packed))
    scale = head_dim ** (-0.5)
    offsets = jnp.arange(block_rows, dtype=jnp.int32)
    group = 0
    window_keys = jnp.concatenate([left_keys, keys], axis=0).reshape(
        2 * blocks_dev, block_rows, head_dim
    )
    window_values = jnp.concatenate([left_values, values], axis=0).reshape(
        2 * blocks_dev, block_rows, head_dim
    )
    query_group = queries.reshape(tok_rows, group_size, head_dim)
    query_feats = feature(query_group, map_query[group])
    reads = jnp.einsum("qhr,rd->qhd", query_feats, states[group], precision=highest)
    mass = jnp.einsum("qhr,r->qh", query_feats, norms[group], precision=highest)
    row_pieces = []
    for local in range(blocks_dev):
        chosen = jnp.concatenate(
            [block_lists[local], jnp.full((1,), blocks_dev + local, jnp.int32)]
        )
        key_rows = jnp.take(window_keys, chosen, axis=0).reshape(-1, head_dim)
        value_rows = jnp.take(window_values, chosen, axis=0).reshape(-1, head_dim)
        positions = (
            ((device - 1) * tok_rows + chosen * block_rows)[:, None] + offsets[None, :]
        ).reshape(-1)
        query_pos = device * tok_rows + local * block_rows + offsets
        valid = (positions[None, :] >= 0) & (positions[None, :] <= query_pos[:, None])
        rows_here = slice(local * block_rows, (local + 1) * block_rows)
        query = query_group[rows_here]
        scores = (
            jnp.einsum("qhd,kd->qhk", query, key_rows, preferred_element_type=jnp.float32) * scale
        )
        scores = jnp.where(valid[:, None, :], scores, -jnp.inf)
        top = jnp.max(scores, axis=2)
        weights = jnp.exp(scores - top[:, :, None])
        total = jnp.sum(weights, axis=2)
        probs = weights.astype(jnp.bfloat16)
        numer = jnp.einsum("qhk,kd->qhd", probs, value_rows, preferred_element_type=jnp.float32)
        damping = jnp.exp(-top) * state_gain[group]
        mixed = (numer + damping[:, :, None] * reads[rows_here]) / (
            total + damping * mass[rows_here]
        )[:, :, None]
        row_pieces.append(mixed.reshape(block_rows, group_size * head_dim).astype(jnp.bfloat16))
    group_cols = jnp.concatenate(row_pieces, axis=0)
    n_tp = lax.axis_size("tp")
    swap = [
        (rows * n_tp + group, ((rows - group) % n_tp) * n_tp + rows)
        for group in range(n_tp)
        for rows in range(n_tp)
    ]
    moved = lax.ppermute(out_weight, ("ctx_0", "tp"), swap)
    depth = moved.shape[0]
    halves = 2
    step = depth // halves
    rows_by_shift = [group_cols] + [
        lax.ppermute(group_cols, "tp", [(i, (i + shift) % n_tp) for i in range(n_tp)])
        for shift in range(1, n_tp)
    ]
    summed = None
    for half in range(halves):
        gathered = lax.all_gather(
            moved[half * step : (half + 1) * step], CTX, axis=1, tiled=True
        )
        if summed is not None:
            gathered, summed = lax.optimization_barrier((gathered, summed))
        width = gathered.shape[1] // n_tp
        for shift in range(n_tp):
            term = jnp.dot(
                rows_by_shift[shift][:, half * step : (half + 1) * step],
                gathered[:, shift * width : (shift + 1) * width],
                preferred_element_type=jnp.float32,
            )
            summed = term if summed is None else summed + term
    return summed.astype(jnp.bfloat16)


def solution(mesh):
    finer = Mesh(mesh.devices.reshape(4, 8, 2, mesh.shape["tp"]), ("ctx_0", "ctx_1", "ctx_2", "tp"))
    placed = (
        P(CTX, "tp"),
        P(CTX, "tp"),
        P(CTX, "tp"),
        P(CTX, "tp"),
        P(CTX, None),
        P("tp", None, None),
        P("tp", None, None),
        P("tp"),
        P("tp", CTX),
    )
    return jax.shard_map(body, mesh=finer, in_specs=placed, out_specs=P(CTX, "tp"), check_vma=False)
```

```python
import jax
import jax.numpy as jnp
from jax import lax
from jax.sharding import Mesh
from jax.sharding import PartitionSpec as P

CTX = ("ctx_0", "ctx_1", "ctx_2")


def passed_along(block, axis, distance):
    devices = range(lax.axis_size(axis))
    route = [(i - distance, i) for i in devices if i - distance in devices]
    return lax.ppermute(block, axis, route)


def neutral_like(shard, identity):
    return jax.tree.map(
        lambda a, e: jnp.broadcast_to(jnp.asarray(e, a.dtype), a.shape), shard, identity
    )


def all_in_one(shard, axis):
    leaves = jax.tree.leaves(shard)
    order = sorted(range(len(leaves)), key=lambda k: -leaves[k].size)
    width = (1, *leaves[order[0]].shape)[-1]
    lines = [
        jnp.pad(leaves[k].reshape(-1), (0, -leaves[k].size % width)).reshape(-1, width)
        for k in order
    ]
    both, at, found = (lax.all_gather(jnp.concatenate(lines), axis), 0, {})
    for k, line in zip(order, lines):
        slab = both[:, at : at + len(line)].reshape(len(both), -1)
        found[k] = slab[:, : leaves[k].size].reshape(-1, *leaves[k].shape)
        at += len(line)
    numbers = iter(range(len(leaves)))
    return jax.tree.map(lambda _: found[next(numbers)], shard)


def carried_in(shard, axes, combine, identity):
    before = start = neutral_like(shard, identity)
    running = shard
    for axis in reversed(axes):
        devices, here = (lax.axis_size(axis), lax.axis_index(axis))
        pieces = all_in_one(
            jax.tree.map(
                lambda part, kind: part.astype(kind), running, (jnp.bfloat16, jnp.bfloat16)
            ),
            axis,
        )
        inside, running = (start, start)
        for k in range(devices):
            passed = k < here
            running = combine(
                running, jax.tree.map(lambda part, own: part[k].astype(own.dtype), pieces, shard)
            )
            inside = jax.tree.map(lambda new, old: jnp.where(passed, new, old), running, inside)
        before = combine(inside, before)
    return before


def feature(inputs, kernel):
    return jax.nn.elu(jnp.dot(inputs, kernel, preferred_element_type=jnp.float32)) + 1.0


def add_pair(earlier, later):
    return (earlier[0] + later[0], earlier[1] + later[1])


def body(queries, keys, values, evicted, block_lists, map_query, map_key, state_gain, out_weight):
    tok_rows = keys.shape[0]
    groups_here = map_key.shape[0]
    head_dim = map_key.shape[1]
    blocks_dev = block_lists.shape[0]
    block_rows = tok_rows // blocks_dev
    group_size = queries.shape[1] // (groups_here * head_dim)
    highest = lax.Precision.HIGHEST
    device = lax.axis_index(CTX)
    width_kv = groups_here * head_dim
    neighbour = passed_along(jnp.concatenate([keys, values], axis=1), CTX, 1)
    left_keys = neighbour[:, :width_kv]
    left_values = neighbour[:, width_kv:]
    group = 0
    key_feats = feature(keys, map_key[group]) * evicted.astype(jnp.float32)
    state_terms = [
        jnp.einsum("tr,th->rh", key_feats, values.astype(jnp.float32), precision=highest)
    ]
    norm_terms = [jnp.sum(key_feats, axis=0)]
    totals = jnp.stack(state_terms)
    counts = jnp.stack(norm_terms)
    states, norms = carried_in(
        (totals, counts), CTX, add_pair, (jnp.zeros_like(totals), jnp.zeros_like(counts))
    )
    scale = head_dim ** (-0.5)
    offsets = jnp.arange(block_rows, dtype=jnp.int32)
    group = 0
    window_keys = jnp.concatenate([left_keys, keys], axis=0).reshape(
        2 * blocks_dev, block_rows, head_dim
    )
    window_values = jnp.concatenate([left_values, values], axis=0).reshape(
        2 * blocks_dev, block_rows, head_dim
    )
    query_group = queries.reshape(tok_rows, group_size, head_dim)
    query_feats = feature(query_group, map_query[group])
    reads = jnp.einsum("qhr,rd->qhd", query_feats, states[group], precision=highest)
    mass = jnp.einsum("qhr,r->qh", query_feats, norms[group], precision=highest)
    row_pieces = []
    for local in range(blocks_dev):
        chosen = jnp.concatenate(
            [block_lists[local], jnp.full((1,), blocks_dev + local, jnp.int32)]
        )
        key_rows = jnp.take(window_keys, chosen, axis=0).reshape(-1, head_dim)
        value_rows = jnp.take(window_values, chosen, axis=0).reshape(-1, head_dim)
        positions = (
            ((device - 1) * tok_rows + chosen * block_rows)[:, None] + offsets[None, :]
        ).reshape(-1)
        query_pos = device * tok_rows + local * block_rows + offsets
        valid = (positions[None, :] >= 0) & (positions[None, :] <= query_pos[:, None])
        rows_here = slice(local * block_rows, (local + 1) * block_rows)
        query = query_group[rows_here]
        scores = (
            jnp.einsum("qhd,kd->qhk", query, key_rows, preferred_element_type=jnp.float32) * scale
        )
        scores = jnp.where(valid[:, None, :], scores, -jnp.inf)
        top = jnp.max(scores, axis=2)
        weights = jnp.exp(scores - top[:, :, None])
        total = jnp.sum(weights, axis=2)
        probs = weights.astype(jnp.bfloat16)
        numer = jnp.einsum("qhk,kd->qhd", probs, value_rows, preferred_element_type=jnp.float32)
        damping = jnp.exp(-top) * state_gain[group]
        mixed = (numer + damping[:, :, None] * reads[rows_here]) / (
            total + damping * mass[rows_here]
        )[:, :, None]
        row_pieces.append(mixed.reshape(block_rows, group_size * head_dim).astype(jnp.bfloat16))
    group_cols = jnp.concatenate(row_pieces, axis=0)
    n_tp = lax.axis_size("tp")
    swap = [
        (rows * n_tp + group, ((rows - group) % n_tp) * n_tp + rows)
        for group in range(n_tp)
        for rows in range(n_tp)
    ]
    moved = lax.ppermute(out_weight, ("ctx_0", "tp"), swap)
    gathered = lax.all_gather(moved, CTX, axis=1, tiled=True)
    width = gathered.shape[1] // n_tp
    rows_by_shift = [group_cols] + [
        lax.ppermute(group_cols, "tp", [(i, (i + shift) % n_tp) for i in range(n_tp)])
        for shift in range(1, n_tp)
    ]
    every_group = jnp.stack(rows_by_shift, axis=1)
    summed = jnp.einsum(
        "tsk,ksn->tn",
        every_group,
        gathered.reshape(gathered.shape[0], n_tp, width),
        preferred_element_type=jnp.float32,
    )
    return summed.astype(jnp.bfloat16)


def solution(mesh):
    finer = Mesh(mesh.devices.reshape(4, 8, 2, mesh.shape["tp"]), ("ctx_0", "ctx_1", "ctx_2", "tp"))
    placed = (
        P(CTX, "tp"),
        P(CTX, "tp"),
        P(CTX, "tp"),
        P(CTX, "tp"),
        P(CTX, None),
        P("tp", None, None),
        P("tp", None, None),
        P("tp"),
        P("tp", CTX),
    )
    return jax.shard_map(body, mesh=finer, in_specs=placed, out_specs=P(CTX, "tp"), check_vma=False)
```

```python
import jax
import jax.numpy as jnp
from jax import lax
from jax.sharding import Mesh
from jax.sharding import PartitionSpec as P

CTX = ("ctx_0", "ctx_1", "ctx_2")


def passed_along(block, axis, distance):
    devices = range(lax.axis_size(axis))
    route = [(i - distance, i) for i in devices if i - distance in devices]
    return lax.ppermute(block, axis, route)


def neutral_like(shard, identity):
    return jax.tree.map(
        lambda a, e: jnp.broadcast_to(jnp.asarray(e, a.dtype), a.shape), shard, identity
    )


def all_in_one(shard, axis):
    leaves = jax.tree.leaves(shard)
    order = sorted(range(len(leaves)), key=lambda k: -leaves[k].size)
    width = (1, *leaves[order[0]].shape)[-1]
    lines = [
        jnp.pad(leaves[k].reshape(-1), (0, -leaves[k].size % width)).reshape(-1, width)
        for k in order
    ]
    both, at, found = (lax.all_gather(jnp.concatenate(lines), axis), 0, {})
    for k, line in zip(order, lines):
        slab = both[:, at : at + len(line)].reshape(len(both), -1)
        found[k] = slab[:, : leaves[k].size].reshape(-1, *leaves[k].shape)
        at += len(line)
    numbers = iter(range(len(leaves)))
    return jax.tree.map(lambda _: found[next(numbers)], shard)


def carried_in(shard, axes, combine, identity):
    before = start = neutral_like(shard, identity)
    running = shard
    for axis in reversed(axes):
        devices, here = (lax.axis_size(axis), lax.axis_index(axis))
        pieces = all_in_one(
            jax.tree.map(
                lambda part, kind: part.astype(kind), running, (jnp.bfloat16, jnp.bfloat16)
            ),
            axis,
        )
        inside, running = (start, start)
        for k in range(devices):
            passed = k < here
            running = combine(
                running, jax.tree.map(lambda part, own: part[k].astype(own.dtype), pieces, shard)
            )
            inside = jax.tree.map(lambda new, old: jnp.where(passed, new, old), running, inside)
        before = combine(inside, before)
    return before


def feature(inputs, kernel):
    return jax.nn.elu(jnp.dot(inputs, kernel, preferred_element_type=jnp.float32)) + 1.0


def add_pair(earlier, later):
    return (earlier[0] + later[0], earlier[1] + later[1])


def body(queries, keys, values, evicted, block_lists, map_query, map_key, state_gain, out_weight):
    tok_rows = keys.shape[0]
    groups_here = map_key.shape[0]
    head_dim = map_key.shape[1]
    blocks_dev = block_lists.shape[0]
    block_rows = tok_rows // blocks_dev
    group_size = queries.shape[1] // (groups_here * head_dim)
    highest = lax.Precision.HIGHEST
    device = lax.axis_index(CTX)
    width_kv = groups_here * head_dim
    neighbour = passed_along(jnp.concatenate([keys, values], axis=1), CTX, 1)
    left_keys = neighbour[:, :width_kv]
    left_values = neighbour[:, width_kv:]
    group = 0
    key_feats = feature(keys, map_key[group]) * evicted.astype(jnp.float32)
    state_terms = [
        jnp.einsum("tr,th->rh", key_feats, values.astype(jnp.float32), precision=highest)
    ]
    norm_terms = [jnp.sum(key_feats, axis=0)]
    totals = jnp.stack(state_terms)
    counts = jnp.stack(norm_terms)
    packed = jnp.concatenate(
        [totals[0], jnp.pad(counts, ((0, 0), (0, totals.shape[2] - counts.shape[1])))], axis=0
    ).astype(jnp.float32)
    before = jnp.zeros_like(packed)
    running = packed
    for axis in reversed(CTX):
        size, here = (lax.axis_size(axis), lax.axis_index(axis))
        whole = running
        for shift in range(1, size):
            arrived = lax.ppermute(running, axis, [(i, (i + shift) % size) for i in range(size)])
            before = before + jnp.where(shift <= here, arrived, 0.0)
            whole = whole + arrived
        running = whole
    states = before[None, : totals.shape[1]]
    norms = before[None, totals.shape[1], : counts.shape[1]]
    scale = head_dim ** (-0.5)
    offsets = jnp.arange(block_rows, dtype=jnp.int32)
    group = 0
    window_keys = jnp.concatenate([left_keys, keys], axis=0).reshape(
        2 * blocks_dev, block_rows, head_dim
    )
    window_values = jnp.concatenate([left_values, values], axis=0).reshape(
        2 * blocks_dev, block_rows, head_dim
    )
    query_group = queries.reshape(tok_rows, group_size, head_dim)
    query_feats = feature(query_group, map_query[group])
    reads = jnp.einsum("qhr,rd->qhd", query_feats, states[group], precision=highest)
    mass = jnp.einsum("qhr,r->qh", query_feats, norms[group], precision=highest)
    row_pieces = []
    for local in range(blocks_dev):
        chosen = jnp.concatenate(
            [block_lists[local], jnp.full((1,), blocks_dev + local, jnp.int32)]
        )
        key_rows = jnp.take(window_keys, chosen, axis=0).reshape(-1, head_dim)
        value_rows = jnp.take(window_values, chosen, axis=0).reshape(-1, head_dim)
        positions = (
            ((device - 1) * tok_rows + chosen * block_rows)[:, None] + offsets[None, :]
        ).reshape(-1)
        query_pos = device * tok_rows + local * block_rows + offsets
        valid = (positions[None, :] >= 0) & (positions[None, :] <= query_pos[:, None])
        rows_here = slice(local * block_rows, (local + 1) * block_rows)
        query = query_group[rows_here]
        scores = (
            jnp.einsum("qhd,kd->qhk", query, key_rows, preferred_element_type=jnp.float32) * scale
        )
        scores = jnp.where(valid[:, None, :], scores, -jnp.inf)
        top = jnp.max(scores, axis=2)
        weights = jnp.exp(scores - top[:, :, None])
        total = jnp.sum(weights, axis=2)
        probs = weights.astype(jnp.bfloat16)
        numer = jnp.einsum("qhk,kd->qhd", probs, value_rows, preferred_element_type=jnp.float32)
        damping = jnp.exp(-top) * state_gain[group]
        mixed = (numer + damping[:, :, None] * reads[rows_here]) / (
            total + damping * mass[rows_here]
        )[:, :, None]
        row_pieces.append(mixed.reshape(block_rows, group_size * head_dim).astype(jnp.bfloat16))
    group_cols = jnp.concatenate(row_pieces, axis=0)
    n_tp = lax.axis_size("tp")
    swap = [
        (rows * n_tp + group, ((rows - group) % n_tp) * n_tp + rows)
        for group in range(n_tp)
        for rows in range(n_tp)
    ]
    moved = lax.ppermute(out_weight, ("ctx_0", "tp"), swap)
    gathered = lax.all_gather(moved, CTX, axis=1, tiled=True)
    width = gathered.shape[1] // n_tp
    summed = None
    for shift in range(n_tp):
        if shift == 0:
            rows_in = group_cols
        else:
            rows_in = lax.ppermute(
                group_cols, "tp", [(i, (i + shift) % n_tp) for i in range(n_tp)]
            )
        term = jnp.dot(
            rows_in,
            gathered[:, shift * width : (shift + 1) * width],
            preferred_element_type=jnp.float32,
        )
        summed = term if summed is None else summed + term
    return summed.astype(jnp.bfloat16)


def solution(mesh):
    finer = Mesh(mesh.devices.reshape(4, 8, 2, mesh.shape["tp"]), ("ctx_0", "ctx_1", "ctx_2", "tp"))
    placed = (
        P(CTX, "tp"),
        P(CTX, "tp"),
        P(CTX, "tp"),
        P(CTX, "tp"),
        P(CTX, None),
        P("tp", None, None),
        P("tp", None, None),
        P("tp"),
        P("tp", CTX),
    )
    return jax.shard_map(body, mesh=finer, in_specs=placed, out_specs=P(CTX, "tp"), check_vma=False)
```

```python
import jax
import jax.numpy as jnp
from jax import lax
from jax.sharding import Mesh
from jax.sharding import PartitionSpec as P

CTX = ("ctx_0", "ctx_1", "ctx_2")


def passed_along(block, axis, distance):
    devices = range(lax.axis_size(axis))
    route = [(i - distance, i) for i in devices if i - distance in devices]
    return lax.ppermute(block, axis, route)


def neutral_like(shard, identity):
    return jax.tree.map(
        lambda a, e: jnp.broadcast_to(jnp.asarray(e, a.dtype), a.shape), shard, identity
    )


def all_in_one(shard, axis):
    leaves = jax.tree.leaves(shard)
    order = sorted(range(len(leaves)), key=lambda k: -leaves[k].size)
    width = (1, *leaves[order[0]].shape)[-1]
    lines = [
        jnp.pad(leaves[k].reshape(-1), (0, -leaves[k].size % width)).reshape(-1, width)
        for k in order
    ]
    both, at, found = (lax.all_gather(jnp.concatenate(lines), axis), 0, {})
    for k, line in zip(order, lines):
        slab = both[:, at : at + len(line)].reshape(len(both), -1)
        found[k] = slab[:, : leaves[k].size].reshape(-1, *leaves[k].shape)
        at += len(line)
    numbers = iter(range(len(leaves)))
    return jax.tree.map(lambda _: found[next(numbers)], shard)


def carried_in(shard, axes, combine, identity):
    before = start = neutral_like(shard, identity)
    running = shard
    for axis in reversed(axes):
        devices, here = (lax.axis_size(axis), lax.axis_index(axis))
        pieces = all_in_one(
            jax.tree.map(
                lambda part, kind: part.astype(kind), running, (jnp.bfloat16, jnp.bfloat16)
            ),
            axis,
        )
        inside, running = (start, start)
        for k in range(devices):
            passed = k < here
            running = combine(
                running, jax.tree.map(lambda part, own: part[k].astype(own.dtype), pieces, shard)
            )
            inside = jax.tree.map(lambda new, old: jnp.where(passed, new, old), running, inside)
        before = combine(inside, before)
    return before


def feature(inputs, kernel):
    return jax.nn.elu(jnp.dot(inputs, kernel, preferred_element_type=jnp.float32)) + 1.0


def add_pair(earlier, later):
    return (earlier[0] + later[0], earlier[1] + later[1])


def body(queries, keys, values, evicted, block_lists, map_query, map_key, state_gain, out_weight):
    tok_rows = keys.shape[0]
    groups_here = map_key.shape[0]
    head_dim = map_key.shape[1]
    blocks_dev = block_lists.shape[0]
    block_rows = tok_rows // blocks_dev
    group_size = queries.shape[1] // (groups_here * head_dim)
    highest = lax.Precision.HIGHEST
    device = lax.axis_index(CTX)
    width_kv = groups_here * head_dim
    neighbour = passed_along(jnp.concatenate([keys, values], axis=1), CTX, 1)
    left_keys = neighbour[:, :width_kv]
    left_values = neighbour[:, width_kv:]
    group = 0
    key_feats = feature(keys, map_key[group]) * evicted.astype(jnp.float32)
    state_terms = [
        jnp.einsum("tr,th->rh", key_feats, values.astype(jnp.float32), precision=highest)
    ]
    norm_terms = [jnp.sum(key_feats, axis=0)]
    totals = jnp.stack(state_terms)
    counts = jnp.stack(norm_terms)
    packed = jnp.concatenate(
        [totals[0], jnp.pad(counts, ((0, 0), (0, totals.shape[2] - counts.shape[1])))], axis=0
    ).astype(jnp.float32)
    before = jnp.zeros_like(packed)
    running = packed
    for axis in reversed(CTX):
        size, here = (lax.axis_size(axis), lax.axis_index(axis))
        whole = running
        for shift in range(1, size):
            arrived = lax.ppermute(running, axis, [(i, (i + shift) % size) for i in range(size)])
            before = before + jnp.where(shift <= here, arrived, 0.0)
            whole = whole + arrived
        running = whole
    states = before[None, : totals.shape[1]]
    norms = before[None, totals.shape[1], : counts.shape[1]]
    scale = head_dim ** (-0.5)
    offsets = jnp.arange(block_rows, dtype=jnp.int32)
    group = 0
    window_keys = jnp.concatenate([left_keys, keys], axis=0).reshape(
        2 * blocks_dev, block_rows, head_dim
    )
    window_values = jnp.concatenate([left_values, values], axis=0).reshape(
        2 * blocks_dev, block_rows, head_dim
    )
    query_group = queries.reshape(tok_rows, group_size, head_dim)
    query_feats = feature(query_group, map_query[group])
    reads = jnp.einsum("qhr,rd->qhd", query_feats, states[group], precision=highest)
    mass = jnp.einsum("qhr,r->qh", query_feats, norms[group], precision=highest)
    row_pieces = []
    for local in range(blocks_dev):
        chosen = jnp.concatenate(
            [block_lists[local], jnp.full((1,), blocks_dev + local, jnp.int32)]
        )
        key_rows = jnp.take(window_keys, chosen, axis=0).reshape(-1, head_dim)
        value_rows = jnp.take(window_values, chosen, axis=0).reshape(-1, head_dim)
        positions = (
            ((device - 1) * tok_rows + chosen * block_rows)[:, None] + offsets[None, :]
        ).reshape(-1)
        query_pos = device * tok_rows + local * block_rows + offsets
        valid = (positions[None, :] >= 0) & (positions[None, :] <= query_pos[:, None])
        rows_here = slice(local * block_rows, (local + 1) * block_rows)
        query = query_group[rows_here]
        scores = (
            jnp.einsum("qhd,kd->qhk", query, key_rows, preferred_element_type=jnp.float32) * scale
        )
        scores = jnp.where(valid[:, None, :], scores, -jnp.inf)
        top = jnp.max(scores, axis=2)
        weights = jnp.exp(scores - top[:, :, None])
        total = jnp.sum(weights, axis=2)
        probs = weights.astype(jnp.bfloat16)
        numer = jnp.einsum("qhk,kd->qhd", probs, value_rows, preferred_element_type=jnp.float32)
        damping = jnp.exp(-top) * state_gain[group]
        mixed = (numer + damping[:, :, None] * reads[rows_here]) / (
            total + damping * mass[rows_here]
        )[:, :, None]
        row_pieces.append(mixed.reshape(block_rows, group_size * head_dim).astype(jnp.bfloat16))
    group_cols = jnp.concatenate(row_pieces, axis=0)
    n_tp = lax.axis_size("tp")
    swap = [
        (rows * n_tp + group, ((rows - group) % n_tp) * n_tp + rows)
        for group in range(n_tp)
        for rows in range(n_tp)
    ]
    moved = lax.ppermute(out_weight, ("ctx_0", "tp"), swap)
    gathered = lax.all_gather(moved, CTX, axis=1, tiled=True)
    width = gathered.shape[1] // n_tp
    rows_by_shift = [group_cols] + [
        lax.ppermute(group_cols, "tp", [(i, (i + shift) % n_tp) for i in range(n_tp)])
        for shift in range(1, n_tp)
    ]
    summed = jnp.einsum(
        "stk,ksn->tn",
        jnp.stack(rows_by_shift),
        gathered.reshape(gathered.shape[0], n_tp, width),
        preferred_element_type=jnp.float32,
    )
    return summed.astype(jnp.bfloat16)


def solution(mesh):
    finer = Mesh(mesh.devices.reshape(4, 8, 2, mesh.shape["tp"]), ("ctx_0", "ctx_1", "ctx_2", "tp"))
    placed = (
        P(CTX, "tp"),
        P(CTX, "tp"),
        P(CTX, "tp"),
        P(CTX, "tp"),
        P(CTX, None),
        P("tp", None, None),
        P("tp", None, None),
        P("tp"),
        P("tp", CTX),
    )
    return jax.shard_map(body, mesh=finer, in_specs=placed, out_specs=P(CTX, "tp"), check_vma=False)
```

```python
import jax
import jax.numpy as jnp
from jax import lax
from jax.sharding import Mesh
from jax.sharding import PartitionSpec as P

CTX = ("ctx_0", "ctx_1", "ctx_2")


def passed_along(block, axis, distance):
    devices = range(lax.axis_size(axis))
    route = [(i - distance, i) for i in devices if i - distance in devices]
    return lax.ppermute(block, axis, route)


def neutral_like(shard, identity):
    return jax.tree.map(
        lambda a, e: jnp.broadcast_to(jnp.asarray(e, a.dtype), a.shape), shard, identity
    )


def all_in_one(shard, axis):
    leaves = jax.tree.leaves(shard)
    order = sorted(range(len(leaves)), key=lambda k: -leaves[k].size)
    width = (1, *leaves[order[0]].shape)[-1]
    lines = [
        jnp.pad(leaves[k].reshape(-1), (0, -leaves[k].size % width)).reshape(-1, width)
        for k in order
    ]
    both, at, found = (lax.all_gather(jnp.concatenate(lines), axis), 0, {})
    for k, line in zip(order, lines):
        slab = both[:, at : at + len(line)].reshape(len(both), -1)
        found[k] = slab[:, : leaves[k].size].reshape(-1, *leaves[k].shape)
        at += len(line)
    numbers = iter(range(len(leaves)))
    return jax.tree.map(lambda _: found[next(numbers)], shard)


def carried_in(shard, axes, combine, identity):
    before = start = neutral_like(shard, identity)
    running = shard
    for axis in reversed(axes):
        devices, here = (lax.axis_size(axis), lax.axis_index(axis))
        pieces = all_in_one(
            jax.tree.map(
                lambda part, kind: part.astype(kind), running, (jnp.bfloat16, jnp.bfloat16)
            ),
            axis,
        )
        inside, running = (start, start)
        for k in range(devices):
            passed = k < here
            running = combine(
                running, jax.tree.map(lambda part, own: part[k].astype(own.dtype), pieces, shard)
            )
            inside = jax.tree.map(lambda new, old: jnp.where(passed, new, old), running, inside)
        before = combine(inside, before)
    return before


def feature(inputs, kernel):
    return jax.nn.elu(jnp.dot(inputs, kernel, preferred_element_type=jnp.float32)) + 1.0


def add_pair(earlier, later):
    return (earlier[0] + later[0], earlier[1] + later[1])


def body(queries, keys, values, evicted, block_lists, map_query, map_key, state_gain, out_weight):
    tok_rows = keys.shape[0]
    groups_here = map_key.shape[0]
    head_dim = map_key.shape[1]
    blocks_dev = block_lists.shape[0]
    block_rows = tok_rows // blocks_dev
    group_size = queries.shape[1] // (groups_here * head_dim)
    highest = lax.Precision.HIGHEST
    device = lax.axis_index(CTX)
    width_kv = groups_here * head_dim
    neighbour = passed_along(jnp.concatenate([keys, values], axis=1), CTX, 1)
    left_keys = neighbour[:, :width_kv]
    left_values = neighbour[:, width_kv:]
    group = 0
    key_feats = feature(keys, map_key[group]) * evicted.astype(jnp.float32)
    state_terms = [
        jnp.einsum("tr,th->rh", key_feats, values.astype(jnp.float32), precision=highest)
    ]
    norm_terms = [jnp.sum(key_feats, axis=0)]
    totals = jnp.stack(state_terms)
    counts = jnp.stack(norm_terms)
    packed = jnp.concatenate(
        [totals[0], jnp.pad(counts, ((0, 0), (0, totals.shape[2] - counts.shape[1])))], axis=0
    ).astype(jnp.float32)
    before = jnp.zeros_like(packed)
    running = packed
    for axis in reversed(CTX):
        size, here = (lax.axis_size(axis), lax.axis_index(axis))
        whole = running
        for shift in range(1, size):
            arrived = lax.ppermute(running, axis, [(i, (i + shift) % size) for i in range(size)])
            before = before + jnp.where(shift <= here, arrived, 0.0)
            whole = whole + arrived
        running = whole
    states = before[None, : totals.shape[1]]
    norms = before[None, totals.shape[1], : counts.shape[1]]
    scale = head_dim ** (-0.5)
    offsets = jnp.arange(block_rows, dtype=jnp.int32)
    group = 0
    window_keys = jnp.concatenate([left_keys, keys], axis=0).reshape(
        2 * blocks_dev, block_rows, head_dim
    )
    window_values = jnp.concatenate([left_values, values], axis=0).reshape(
        2 * blocks_dev, block_rows, head_dim
    )
    query_group = queries.reshape(tok_rows, group_size, head_dim)
    query_feats = feature(query_group, map_query[group])
    reads = jnp.einsum("qhr,rd->qhd", query_feats, states[group], precision=highest)
    mass = jnp.einsum("qhr,r->qh", query_feats, norms[group], precision=highest)
    row_pieces = []
    for local in range(blocks_dev):
        chosen = jnp.concatenate(
            [block_lists[local], jnp.full((1,), blocks_dev + local, jnp.int32)]
        )
        key_rows = jnp.take(window_keys, chosen, axis=0).reshape(-1, head_dim)
        value_rows = jnp.take(window_values, chosen, axis=0).reshape(-1, head_dim)
        positions = (
            ((device - 1) * tok_rows + chosen * block_rows)[:, None] + offsets[None, :]
        ).reshape(-1)
        query_pos = device * tok_rows + local * block_rows + offsets
        valid = (positions[None, :] >= 0) & (positions[None, :] <= query_pos[:, None])
        rows_here = slice(local * block_rows, (local + 1) * block_rows)
        query = query_group[rows_here]
        scores = (
            jnp.einsum("qhd,kd->qhk", query, key_rows, preferred_element_type=jnp.float32) * scale
        )
        scores = jnp.where(valid[:, None, :], scores, -jnp.inf)
        top = jnp.max(scores, axis=2)
        weights = jnp.exp(scores - top[:, :, None])
        total = jnp.sum(weights, axis=2)
        probs = weights.astype(jnp.bfloat16)
        numer = jnp.einsum("qhk,kd->qhd", probs, value_rows, preferred_element_type=jnp.float32)
        damping = jnp.exp(-top) * state_gain[group]
        mixed = (numer + damping[:, :, None] * reads[rows_here]) / (
            total + damping * mass[rows_here]
        )[:, :, None]
        row_pieces.append(mixed.reshape(block_rows, group_size * head_dim).astype(jnp.bfloat16))
    group_cols = jnp.concatenate(row_pieces, axis=0)
    n_tp = lax.axis_size("tp")
    swap = [
        (rows * n_tp + group, ((rows - group) % n_tp) * n_tp + rows)
        for group in range(n_tp)
        for rows in range(n_tp)
    ]
    moved = lax.ppermute(out_weight, ("ctx_0", "tp"), swap)
    gathered = lax.all_gather(moved, CTX, axis=1, tiled=True)
    width = gathered.shape[1] // n_tp
    summed = None
    for shift in range(n_tp):
        if shift == 0:
            rows_in = group_cols
        else:
            rows_in = lax.ppermute(
                group_cols, "tp", [(i, (i + shift) % n_tp) for i in range(n_tp)]
            )
        term = jnp.dot(
            rows_in,
            gathered[:, shift * width : (shift + 1) * width],
            preferred_element_type=jnp.bfloat16,
        ).astype(jnp.float32)
        summed = term if summed is None else summed + term
    return summed.astype(jnp.bfloat16)


def solution(mesh):
    finer = Mesh(mesh.devices.reshape(4, 8, 2, mesh.shape["tp"]), ("ctx_0", "ctx_1", "ctx_2", "tp"))
    placed = (
        P(CTX, "tp"),
        P(CTX, "tp"),
        P(CTX, "tp"),
        P(CTX, "tp"),
        P(CTX, None),
        P("tp", None, None),
        P("tp", None, None),
        P("tp"),
        P("tp", CTX),
    )
    return jax.shard_map(body, mesh=finer, in_specs=placed, out_specs=P(CTX, "tp"), check_vma=False)
```

```python
import jax
import jax.numpy as jnp
from jax import lax
from jax.sharding import Mesh
from jax.sharding import PartitionSpec as P

CTX = ("ctx_0", "ctx_1", "ctx_2")


def passed_along(block, axis, distance):
    devices = range(lax.axis_size(axis))
    route = [(i - distance, i) for i in devices if i - distance in devices]
    return lax.ppermute(block, axis, route)


def neutral_like(shard, identity):
    return jax.tree.map(
        lambda a, e: jnp.broadcast_to(jnp.asarray(e, a.dtype), a.shape), shard, identity
    )


def all_in_one(shard, axis):
    leaves = jax.tree.leaves(shard)
    order = sorted(range(len(leaves)), key=lambda k: -leaves[k].size)
    width = (1, *leaves[order[0]].shape)[-1]
    lines = [
        jnp.pad(leaves[k].reshape(-1), (0, -leaves[k].size % width)).reshape(-1, width)
        for k in order
    ]
    both, at, found = (lax.all_gather(jnp.concatenate(lines), axis), 0, {})
    for k, line in zip(order, lines):
        slab = both[:, at : at + len(line)].reshape(len(both), -1)
        found[k] = slab[:, : leaves[k].size].reshape(-1, *leaves[k].shape)
        at += len(line)
    numbers = iter(range(len(leaves)))
    return jax.tree.map(lambda _: found[next(numbers)], shard)


def carried_in(shard, axes, combine, identity):
    before = start = neutral_like(shard, identity)
    running = shard
    for axis in reversed(axes):
        devices, here = (lax.axis_size(axis), lax.axis_index(axis))
        pieces = all_in_one(
            jax.tree.map(
                lambda part, kind: part.astype(kind), running, (jnp.bfloat16, jnp.bfloat16)
            ),
            axis,
        )
        inside, running = (start, start)
        for k in range(devices):
            passed = k < here
            running = combine(
                running, jax.tree.map(lambda part, own: part[k].astype(own.dtype), pieces, shard)
            )
            inside = jax.tree.map(lambda new, old: jnp.where(passed, new, old), running, inside)
        before = combine(inside, before)
    return before


def feature(inputs, kernel):
    return jax.nn.elu(jnp.dot(inputs, kernel, preferred_element_type=jnp.float32)) + 1.0


def add_pair(earlier, later):
    return (earlier[0] + later[0], earlier[1] + later[1])


def body(queries, keys, values, evicted, block_lists, map_query, map_key, state_gain, out_weight):
    tok_rows = keys.shape[0]
    groups_here = map_key.shape[0]
    head_dim = map_key.shape[1]
    blocks_dev = block_lists.shape[0]
    block_rows = tok_rows // blocks_dev
    group_size = queries.shape[1] // (groups_here * head_dim)
    highest = lax.Precision.HIGHEST
    device = lax.axis_index(CTX)
    width_kv = groups_here * head_dim
    neighbour = passed_along(jnp.concatenate([keys, values], axis=1), CTX, 1)
    left_keys = neighbour[:, :width_kv]
    left_values = neighbour[:, width_kv:]
    group = 0
    key_feats = feature(keys, map_key[group]) * evicted.astype(jnp.float32)
    state_terms = [
        jnp.einsum("tr,th->rh", key_feats, values.astype(jnp.float32), precision=highest)
    ]
    norm_terms = [jnp.sum(key_feats, axis=0)]
    totals = jnp.stack(state_terms)
    counts = jnp.stack(norm_terms)
    packed = jnp.concatenate(
        [totals[0], jnp.pad(counts, ((0, 0), (0, totals.shape[2] - counts.shape[1])))], axis=0
    ).astype(jnp.float32)
    before = jnp.zeros_like(packed)
    running = packed
    for axis in reversed(CTX[1:]):
        size, here = (lax.axis_size(axis), lax.axis_index(axis))
        whole = running
        for shift in range(1, size):
            arrived = lax.ppermute(running, axis, [(i, (i + shift) % size) for i in range(size)])
            before = before + jnp.where(shift <= here, arrived, 0.0)
            whole = whole + arrived
        running = whole
    size = lax.axis_size(CTX[0])
    upto = running
    shift = 1
    while shift < size:
        upto = upto + lax.ppermute(upto, CTX[0], [(i, i + shift) for i in range(size - shift)])
        shift *= 2
    before = before + (upto - running)
    states = before[None, : totals.shape[1]]
    norms = before[None, totals.shape[1], : counts.shape[1]]
    scale = head_dim ** (-0.5)
    offsets = jnp.arange(block_rows, dtype=jnp.int32)
    group = 0
    window_keys = jnp.concatenate([left_keys, keys], axis=0).reshape(
        2 * blocks_dev, block_rows, head_dim
    )
    window_values = jnp.concatenate([left_values, values], axis=0).reshape(
        2 * blocks_dev, block_rows, head_dim
    )
    query_group = queries.reshape(tok_rows, group_size, head_dim)
    query_feats = feature(query_group, map_query[group])
    reads = jnp.einsum("qhr,rd->qhd", query_feats, states[group], precision=highest)
    mass = jnp.einsum("qhr,r->qh", query_feats, norms[group], precision=highest)
    row_pieces = []
    for local in range(blocks_dev):
        chosen = jnp.concatenate(
            [block_lists[local], jnp.full((1,), blocks_dev + local, jnp.int32)]
        )
        key_rows = jnp.take(window_keys, chosen, axis=0).reshape(-1, head_dim)
        value_rows = jnp.take(window_values, chosen, axis=0).reshape(-1, head_dim)
        positions = (
            ((device - 1) * tok_rows + chosen * block_rows)[:, None] + offsets[None, :]
        ).reshape(-1)
        query_pos = device * tok_rows + local * block_rows + offsets
        valid = (positions[None, :] >= 0) & (positions[None, :] <= query_pos[:, None])
        rows_here = slice(local * block_rows, (local + 1) * block_rows)
        query = query_group[rows_here]
        scores = (
            jnp.einsum("qhd,kd->qhk", query, key_rows, preferred_element_type=jnp.float32) * scale
        )
        scores = jnp.where(valid[:, None, :], scores, -jnp.inf)
        top = jnp.max(scores, axis=2)
        weights = jnp.exp(scores - top[:, :, None])
        total = jnp.sum(weights, axis=2)
        probs = weights.astype(jnp.bfloat16)
        numer = jnp.einsum("qhk,kd->qhd", probs, value_rows, preferred_element_type=jnp.float32)
        damping = jnp.exp(-top) * state_gain[group]
        mixed = (numer + damping[:, :, None] * reads[rows_here]) / (
            total + damping * mass[rows_here]
        )[:, :, None]
        row_pieces.append(mixed.reshape(block_rows, group_size * head_dim).astype(jnp.bfloat16))
    group_cols = jnp.concatenate(row_pieces, axis=0)
    n_tp = lax.axis_size("tp")
    swap = [
        (rows * n_tp + group, ((rows - group) % n_tp) * n_tp + rows)
        for group in range(n_tp)
        for rows in range(n_tp)
    ]
    moved = lax.ppermute(out_weight, ("ctx_0", "tp"), swap)
    gathered = lax.all_gather(moved, CTX, axis=1, tiled=True)
    width = gathered.shape[1] // n_tp
    summed = None
    for shift in range(n_tp):
        if shift == 0:
            rows_in = group_cols
        else:
            rows_in = lax.ppermute(
                group_cols, "tp", [(i, (i + shift) % n_tp) for i in range(n_tp)]
            )
        term = jnp.dot(
            rows_in,
            gathered[:, shift * width : (shift + 1) * width],
            preferred_element_type=jnp.float32,
        )
        summed = term if summed is None else summed + term
    return summed.astype(jnp.bfloat16)


def solution(mesh):
    finer = Mesh(mesh.devices.reshape(4, 8, 2, mesh.shape["tp"]), ("ctx_0", "ctx_1", "ctx_2", "tp"))
    placed = (
        P(CTX, "tp"),
        P(CTX, "tp"),
        P(CTX, "tp"),
        P(CTX, "tp"),
        P(CTX, None),
        P("tp", None, None),
        P("tp", None, None),
        P("tp"),
        P("tp", CTX),
    )
    return jax.shard_map(body, mesh=finer, in_specs=placed, out_specs=P(CTX, "tp"), check_vma=False)
```

```python
import jax
import jax.numpy as jnp
from jax import lax
from jax.sharding import Mesh
from jax.sharding import PartitionSpec as P

CTX = ("ctx_0", "ctx_1", "ctx_2")


def passed_along(block, axis, distance):
    devices = range(lax.axis_size(axis))
    route = [(i - distance, i) for i in devices if i - distance in devices]
    return lax.ppermute(block, axis, route)


def neutral_like(shard, identity):
    return jax.tree.map(
        lambda a, e: jnp.broadcast_to(jnp.asarray(e, a.dtype), a.shape), shard, identity
    )


def all_in_one(shard, axis):
    leaves = jax.tree.leaves(shard)
    order = sorted(range(len(leaves)), key=lambda k: -leaves[k].size)
    width = (1, *leaves[order[0]].shape)[-1]
    lines = [
        jnp.pad(leaves[k].reshape(-1), (0, -leaves[k].size % width)).reshape(-1, width)
        for k in order
    ]
    both, at, found = (lax.all_gather(jnp.concatenate(lines), axis), 0, {})
    for k, line in zip(order, lines):
        slab = both[:, at : at + len(line)].reshape(len(both), -1)
        found[k] = slab[:, : leaves[k].size].reshape(-1, *leaves[k].shape)
        at += len(line)
    numbers = iter(range(len(leaves)))
    return jax.tree.map(lambda _: found[next(numbers)], shard)


def carried_in(shard, axes, combine, identity):
    before = start = neutral_like(shard, identity)
    running = shard
    for axis in reversed(axes):
        devices, here = (lax.axis_size(axis), lax.axis_index(axis))
        pieces = all_in_one(
            jax.tree.map(
                lambda part, kind: part.astype(kind), running, (jnp.bfloat16, jnp.bfloat16)
            ),
            axis,
        )
        inside, running = (start, start)
        for k in range(devices):
            passed = k < here
            running = combine(
                running, jax.tree.map(lambda part, own: part[k].astype(own.dtype), pieces, shard)
            )
            inside = jax.tree.map(lambda new, old: jnp.where(passed, new, old), running, inside)
        before = combine(inside, before)
    return before


def feature(inputs, kernel):
    return jax.nn.elu(jnp.dot(inputs, kernel, preferred_element_type=jnp.float32)) + 1.0


def add_pair(earlier, later):
    return (earlier[0] + later[0], earlier[1] + later[1])


def body(queries, keys, values, evicted, block_lists, map_query, map_key, state_gain, out_weight):
    tok_rows = keys.shape[0]
    groups_here = map_key.shape[0]
    head_dim = map_key.shape[1]
    blocks_dev = block_lists.shape[0]
    block_rows = tok_rows // blocks_dev
    group_size = queries.shape[1] // (groups_here * head_dim)
    highest = lax.Precision.HIGHEST
    device = lax.axis_index(CTX)
    width_kv = groups_here * head_dim
    neighbour = passed_along(jnp.concatenate([keys, values], axis=1), CTX, 1)
    left_keys = neighbour[:, :width_kv]
    left_values = neighbour[:, width_kv:]
    group = 0
    key_feats = feature(keys, map_key[group]) * evicted.astype(jnp.float32)
    state_terms = [
        jnp.einsum("tr,th->rh", key_feats, values.astype(jnp.float32), precision=highest)
    ]
    norm_terms = [jnp.sum(key_feats, axis=0)]
    totals = jnp.stack(state_terms)
    counts = jnp.stack(norm_terms)
    packed = jnp.concatenate(
        [totals[0], jnp.pad(counts, ((0, 0), (0, totals.shape[2] - counts.shape[1])))], axis=0
    ).astype(jnp.float32)
    before = jnp.zeros_like(packed)
    running = packed
    for axis in reversed(CTX):
        size, here = (lax.axis_size(axis), lax.axis_index(axis))
        whole = running
        for shift in range(1, size):
            arrived = lax.ppermute(running, axis, [(i, (i + shift) % size) for i in range(size)])
            before = before + jnp.where(shift <= here, arrived, 0.0)
            whole = whole + arrived
        running = whole
    states = before[None, : totals.shape[1]]
    norms = before[None, totals.shape[1], : counts.shape[1]]
    scale = head_dim ** (-0.5)
    offsets = jnp.arange(block_rows, dtype=jnp.int32)
    group = 0
    window_keys = jnp.concatenate([left_keys, keys], axis=0).reshape(
        2 * blocks_dev, block_rows, head_dim
    )
    window_values = jnp.concatenate([left_values, values], axis=0).reshape(
        2 * blocks_dev, block_rows, head_dim
    )
    query_group = queries.reshape(tok_rows, group_size, head_dim)
    query_feats = feature(query_group, map_query[group])
    reads = jnp.einsum("qhr,rd->qhd", query_feats, states[group], precision=highest)
    mass = jnp.einsum("qhr,r->qh", query_feats, norms[group], precision=highest)
    row_pieces = []
    for local in range(blocks_dev):
        chosen = jnp.concatenate(
            [block_lists[local], jnp.full((1,), blocks_dev + local, jnp.int32)]
        )
        key_rows = jnp.take(window_keys, chosen, axis=0).reshape(-1, head_dim)
        value_rows = jnp.take(window_values, chosen, axis=0).reshape(-1, head_dim)
        positions = (
            ((device - 1) * tok_rows + chosen * block_rows)[:, None] + offsets[None, :]
        ).reshape(-1)
        query_pos = device * tok_rows + local * block_rows + offsets
        valid = (positions[None, :] >= 0) & (positions[None, :] <= query_pos[:, None])
        rows_here = slice(local * block_rows, (local + 1) * block_rows)
        query = query_group[rows_here]
        scores = (
            jnp.einsum("qhd,kd->qhk", query, key_rows, preferred_element_type=jnp.float32) * scale
        )
        scores = jnp.where(valid[:, None, :], scores, -jnp.inf)
        top = jnp.max(scores, axis=2)
        weights = jnp.exp(scores - top[:, :, None])
        total = jnp.sum(weights, axis=2)
        probs = weights.astype(jnp.bfloat16)
        numer = jnp.einsum("qhk,kd->qhd", probs, value_rows, preferred_element_type=jnp.float32)
        damping = jnp.exp(-top) * state_gain[group]
        mixed = (numer + damping[:, :, None] * reads[rows_here]) / (
            total + damping * mass[rows_here]
        )[:, :, None]
        row_pieces.append(mixed.reshape(block_rows, group_size * head_dim).astype(jnp.bfloat16))
    group_cols = jnp.concatenate(row_pieces, axis=0)
    n_tp = lax.axis_size("tp")
    swap = [
        (rows * n_tp + group, group * n_tp + rows)
        for group in range(n_tp)
        for rows in range(n_tp)
    ]
    moved = lax.ppermute(out_weight, ("ctx_0", "tp"), swap)
    gathered = lax.all_gather(moved, CTX, axis=1, tiled=True)
    width = gathered.shape[1] // n_tp
    every_group = lax.all_to_all(
        jnp.broadcast_to(group_cols, (n_tp, *group_cols.shape)), "tp", 0, 0
    )
    summed = None
    for group in range(n_tp):
        term = jnp.dot(
            every_group[group],
            gathered[:, group * width : (group + 1) * width],
            preferred_element_type=jnp.float32,
        )
        summed = term if summed is None else summed + term
    return summed.astype(jnp.bfloat16)


def solution(mesh):
    finer = Mesh(mesh.devices.reshape(4, 8, 2, mesh.shape["tp"]), ("ctx_0", "ctx_1", "ctx_2", "tp"))
    placed = (
        P(CTX, "tp"),
        P(CTX, "tp"),
        P(CTX, "tp"),
        P(CTX, "tp"),
        P(CTX, None),
        P("tp", None, None),
        P("tp", None, None),
        P("tp"),
        P("tp", CTX),
    )
    return jax.shard_map(body, mesh=finer, in_specs=placed, out_specs=P(CTX, "tp"), check_vma=False)
```
